256 devices in a mesh: expert: 16 (over y, x), tensor: 8 (over z), dp: 2 (over core).
Axes of the slice: x: 4, y: 4, z: 8, core: 2. Of those that a mesh axis runs over, the one named last changes fastest.
Arguments:
- out_grad: bfloat16 [16384, 2048], P(('expert', 'dp'), 'tensor'), may hold values from -1.5 to 1.5
- expert_ids: int32 [16384, 2], P(('expert', 'dp')), may hold values from 0 to 31, all different within a row; in each aligned block of 512 rows (0 to 511, 512 to 1023, ...) at most 36 rows name the same one
- gate_weights: float32 [16384, 2], P(('expert', 'dp')), may hold values from 0.05 to 1
- keep: int32 [16384, 2], P(('expert', 'dp')), may hold values 0 or 1
- hidden_act: bfloat16 [32, 1152, 7168], P('expert', 'dp', 'tensor'), may hold values from -3 to 3
- down_weight: bfloat16 [32, 7168, 2048], P('expert', 'tensor', 'dp'), may hold values from -0.0625 to 0.0625
Outputs:
- grad_down: bfloat16 [32, 7168, 2048], P('expert', 'tensor', 'dp')
- grad_hidden: bfloat16 [32, 1152, 7168], P('expert', 'dp', 'tensor')
- gate_grad: float32 [16384, 2], P(('expert', 'dp'))
The draws below stay inside these ranges and needn't reach their ends.
Inputs may be any that keep to these rules, and one draw needn't show every extreme that they name: `expert_ids`: each row names two different experts; among the 512 rows of one device no expert is named more than 36 times, and in every draw some device names some expert exactly 36 times.
All inputs are finite; a program needn't handle non-finite values. No bound on the sum of `keep` on one device may be relied on, other than what follows from the above.
Results may differ from the reference program's by a relative error of at most 0.0064.
Values may be sent and summed in bfloat16 or wider, within the bound.
No kernel may reach another device: no remote copies, remote signals or barrier semaphores. Data moves between devices by JAX's collectives and lax.ppermute only.
A program may use at most 128 MiB of HBM per device.

```python
import math
import jax
import jax.numpy as jnp
import numpy as np
from jax import lax

D = 2048
FF = 7168
EXPERTS = 32
TOK_DEV = 512
CAP = 36
SLOTS = 576
TOKENS = 16384
N_EXPERT = 16
N_DP = 2


def place_ends(entries, stream_key, low, high):
    longest = entries.shape.index(max(entries.shape))
    spots = []
    for shift in (0, 1):
        where = [jax.random.randint(jax.random.fold_in(stream_key, axis), (), 0, length) for axis, length in enumerate(entries.shape)]
        where[longest] = (where[longest] + shift) % entries.shape[longest]
        spots.append(tuple(where))
    return entries.at[spots[0]].set(low).at[spots[1]].set(high)


def block_levels(rng, dims, shards, smallest, largest):
    gain, own = 1.0, jax.random.fold_in(rng, 6)
    for dim, parts in shards:
        draws = jnp.exp(jax.random.uniform(jax.random.fold_in(own, dim), (parts,), jnp.float32, smallest / len(shards), largest / len(shards)))
        gain = gain * jnp.repeat(draws, dims[dim] // parts).reshape([-1 if axis == dim else 1 for axis in range(len(dims))])
    return gain


def routed_block(own_key, own, number, rows, count, top, most, slope):
    order = jax.random.permutation(own_key, count)
    crowded, common = portions_of(count, rows * top, most, slope, True), portions_of(count, rows * top, most, slope, False)
    places = jnp.arange(count)

    def named(sizes, offset_by):
        used = int((sizes > 0).sum())
        fixed = max(1, used // 4)
        moved = fixed + (places - fixed + offset_by * (used - fixed)) % max(1, count - fixed)
        return jnp.zeros((count,), jnp.int32).at[order[jnp.where(places < fixed, places, moved)]].set(jnp.asarray(sizes, jnp.int32))

    sizes = jnp.where(number % 4 == 0, named(crowded, number // 4), named(common, number - number // 4 - 1))
    mixed = jax.random.permutation(jax.random.fold_in(own, 3), count)
    source_of, taker = mixed[0:count // 2 * 2:2], mixed[1:count // 2 * 2:2]
    room = jnp.minimum(sizes[source_of] - 1, most - sizes[taker]) // 2
    room = jnp.where((source_of == order[0]) | (taker == order[0]) | (sizes[taker] == 0), 0, jnp.maximum(room, 0))
    moved = jax.random.randint(jax.random.fold_in(own, 4), (count // 2,), 0, 1 << 20) % (room + 1)
    sizes = sizes.at[source_of].add(-moved).at[taker].add(moved)
    members = jnp.searchsorted(jnp.cumsum(sizes), jnp.arange(rows * top), side="right").astype(jnp.int32)
    listing = members.reshape(top, rows).T
    listing = listing[jax.random.permutation(jax.random.fold_in(own, 1), rows)]
    offset_by = jax.random.randint(jax.random.fold_in(own, 2), (rows, 1), 0, top)
    return jnp.take_along_axis(listing, (jnp.arange(top)[None, :] + offset_by) % top, axis=1)


def portions_of(number_of, total, bound, slope, full):
    portions = [(1 << 20) // math.isqrt(rank ** slope) + 1 for rank in range(1, number_of + 1)]
    largest = bound if full else min(bound, max(-(-total // number_of), total * portions[0] // sum(portions)))
    least = 1 if total - largest >= number_of - 1 else 0
    holding, rest = [largest] + [least] * (number_of - 1), total - largest - least * (number_of - 1)
    while rest > 0:
        candidates = [i for i in range(1, number_of) if holding[i] < largest] or [i for i in range(1, number_of) if holding[i] < bound]
        pool, remaining = sum([portions[i] for i in candidates]), rest
        for i in candidates:
            extra = min(bound - holding[i], max(1, remaining * portions[i] // pool), rest)
            holding[i] = holding[i] + extra
            rest = rest - extra
    return np.array(holding)


def centred(rng, shape, width, bound, pieces=(), kind=jnp.bfloat16):
    loudness = block_levels(rng, shape, pieces, -0.22, 0.18) if pieces else 1.0
    entries = jax.random.normal(rng, shape, jnp.float32) * width * loudness
    return jnp.minimum(jnp.maximum(entries, -bound), bound).astype(kind)


def setup_inputs(seed: int = 0) -> dict:
    arg_keys = jax.random.split(jax.random.key(seed), 7)
    out_grad = centred(arg_keys[0], (TOKENS, D), 0.25, 1.5, ((0, 32), (1, 8)))
    expert_ids_keys = jax.random.split(jax.random.fold_in(arg_keys[1], 1), TOKENS // TOK_DEV)
    expert_ids_turns = jax.random.permutation(jax.random.fold_in(arg_keys[1], 3), TOKENS // TOK_DEV)
    expert_ids = jax.vmap(lambda own, number: routed_block(jax.random.fold_in(arg_keys[1], 2), own, number, TOK_DEV, EXPERTS, 2, CAP, 2))(expert_ids_keys, expert_ids_turns).reshape((TOKENS, 2))
    gate_weights = jnp.clip(jnp.exp(math.log(1.0) - 2.9957323 * jax.random.uniform(arg_keys[2], (TOKENS, 2), jnp.float32) ** block_levels(arg_keys[2], (TOKENS, 2), ((0, 32),), -0.2, 0.2)), 0.05, 1.0)
    keep = place_ends((jax.random.randint(arg_keys[3], (TOKENS, 2), 0, 8) < 7).astype(jnp.int32), jax.random.fold_in(arg_keys[3], 1), 0, 1)
    hidden_act = centred(arg_keys[4], (EXPERTS, N_DP * SLOTS, FF), 0.5, 3.0, ((0, 16), (1, 2), (2, 8)))
    down_weight = centred(arg_keys[5], (EXPERTS, FF, D), FF ** -0.5, 0.0625, ((0, 16), (1, 8), (2, 2)))
    return {"out_grad": out_grad, "expert_ids": expert_ids, "gate_weights": gate_weights, "keep": keep, "hidden_act": hidden_act, "down_weight": down_weight}


def reference(out_grad, expert_ids, gate_weights, keep, hidden_act, down_weight):
    blocks = N_EXPERT * N_DP
    chosen = expert_ids.reshape(blocks, TOK_DEV * 2)
    onehot = (chosen[:, :, None] == jnp.arange(EXPERTS, dtype=jnp.int32)[None, None, :]).astype(jnp.int32)
    ranking = jnp.cumsum(onehot, axis=1) - onehot
    slot_in = jnp.sum(ranking * onehot, axis=2).astype(jnp.int32)
    block_id = jnp.arange(blocks, dtype=jnp.int32)[:, None]
    source = block_id // N_DP
    replica = block_id % N_DP
    dest_row = (replica * SLOTS + source * CAP + slot_in).reshape(-1).astype(jnp.int32)
    dest_expert = chosen.reshape(-1).astype(jnp.int32)
    repeated = jnp.repeat(out_grad, 2, axis=0)
    routed = jnp.zeros((EXPERTS, N_DP * SLOTS, D), jnp.bfloat16).at[dest_expert, dest_row].set(repeated)
    kept_mask = keep.reshape(-1).astype(jnp.float32)
    scale_flat = (gate_weights.reshape(-1) * kept_mask).astype(jnp.bfloat16)
    slot_scale = jnp.zeros((EXPERTS, N_DP * SLOTS), jnp.bfloat16).at[dest_expert, dest_row].set(scale_flat)

    def per_expert(expert_index):
        slot_rows = routed[expert_index]
        slot_weight = slot_scale[expert_index].astype(jnp.float32)
        hidden_rows = hidden_act[expert_index]
        weight_matrix = down_weight[expert_index]
        backprop = jnp.dot(slot_rows, weight_matrix.T, preferred_element_type=jnp.float32)
        grad_rows = (slot_weight[:, None] * backprop).astype(jnp.bfloat16)
        scores = jnp.sum(backprop * hidden_rows.astype(jnp.float32), axis=1)
        scaled = (slot_weight[:, None] * slot_rows.astype(jnp.float32)).astype(jnp.bfloat16)
        summed = jnp.zeros((FF, D), jnp.float32)
        for replica_idx in range(N_DP):
            first_row = replica_idx * SLOTS
            dp_term = jnp.dot(hidden_rows[first_row:first_row + SLOTS].T, scaled[first_row:first_row + SLOTS], preferred_element_type=jnp.float32).astype(jnp.bfloat16)
            dp_term = lax.optimization_barrier(dp_term)
            summed = summed + dp_term.astype(jnp.float32)
        return grad_rows, summed.astype(jnp.bfloat16), scores

    grad_hidden, grad_down, scores = lax.map(per_expert, jnp.arange(EXPERTS, dtype=jnp.int32))
    gate_grad = (scores[dest_expert, dest_row] * kept_mask).reshape(TOKENS, 2)
    return grad_down, grad_hidden, gate_grad
```

```python
import jax
import jax.numpy as jnp
from jax import lax
from jax.sharding import PartitionSpec as P


def from_partner(value, axis, stride):
    mask = 2**stride
    pairs = [(source, source ^ mask) for source in range(lax.axis_size(axis))]
    return lax.ppermute(value, axis, pairs)


def body(out_grad, expert_ids, gate_weights, keep, hidden_act, down_weight):
    token_count = out_grad.shape[0]
    experts = lax.axis_size("expert")
    local_experts = hidden_act.shape[0]
    total_experts = experts * local_experts
    slot_count = hidden_act.shape[1]
    capacity = slot_count // experts
    places = total_experts * capacity
    chosen = expert_ids.reshape(-1)
    count = chosen.shape[0]
    onehot = chosen[:, None] == jnp.arange(total_experts, dtype=jnp.int32)[None, :]
    earlier = (
        jnp.arange(count, dtype=jnp.int32)[:, None] > jnp.arange(count, dtype=jnp.int32)[None, :]
    ).astype(jnp.bfloat16)
    ranking = jnp.dot(earlier, onehot.astype(jnp.bfloat16), preferred_element_type=jnp.float32)
    slot = jnp.sum(jnp.where(onehot, ranking, 0.0), axis=1).astype(jnp.int32)
    position = chosen * capacity + slot
    pos2 = position.reshape(token_count, 2)
    iota_p = jnp.arange(places, dtype=jnp.int32)[:, None]
    pick0 = pos2[None, :, 0] == iota_p
    pick1 = pos2[None, :, 1] == iota_p
    placing = (pick0 | pick1).astype(jnp.bfloat16)
    kept = keep.astype(jnp.float32)
    scale = (gate_weights * kept).astype(jnp.bfloat16)
    slot_scale = (
        jnp.dot(pick0.astype(jnp.bfloat16), scale[:, 0], preferred_element_type=jnp.float32)
        + jnp.dot(pick1.astype(jnp.bfloat16), scale[:, 1], preferred_element_type=jnp.float32)
    ).astype(jnp.bfloat16).reshape(experts, local_experts, capacity)
    gathered = lax.all_gather(out_grad, "tensor", axis=1, tiled=True)
    outgoing = jnp.dot(placing, gathered, preferred_element_type=jnp.float32).astype(jnp.bfloat16)
    arrived, arrived_scale = (
        lax.all_to_all(
            outgoing.reshape(experts, local_experts, capacity, -1),
            "expert",
            split_axis=0,
            concat_axis=2,
            tiled=True,
        ),
        lax.all_to_all(slot_scale, "expert", split_axis=0, concat_axis=2, tiled=True),
    )
    routed = arrived.reshape(local_experts, slot_count, -1)
    weight = arrived_scale.reshape(local_experts, slot_count).astype(jnp.float32)
    backprop = lax.dot_general(
        routed,
        lax.all_gather(down_weight, "dp", axis=2, tiled=True),
        (((2,), (2,)), ((0,), (0,))),
        preferred_element_type=jnp.float32,
    )
    grad_hidden = (weight[:, :, None] * backprop).astype(jnp.bfloat16)
    partial_score = jnp.sum(backprop * hidden_act.astype(jnp.float32), axis=2)
    scores = jnp.sum(lax.all_gather(partial_score, "tensor", axis=0, tiled=False), axis=0)
    returned = lax.all_to_all(
        scores.reshape(local_experts, experts, capacity),
        "expert",
        split_axis=1,
        concat_axis=0,
        tiled=True,
    ).reshape(-1)
    picked = jnp.sum(
        jnp.where(position[:, None] == iota_p[None, :, 0], returned[None, :], 0.0), axis=1
    )
    gate_grad = picked.reshape(token_count, 2) * kept
    scaled = (weight[:, :, None] * routed.astype(jnp.float32)).astype(jnp.bfloat16)
    contract_rows = (((1,), (1,)), ((0,), (0,)))
    half_width = scaled.shape[2] // 2
    dp_index = lax.axis_index("dp")
    own_cols = lax.dynamic_slice_in_dim(scaled, dp_index * half_width, half_width, 2)
    theirs = lax.dynamic_slice_in_dim(scaled, (1 - dp_index) * half_width, half_width, 2)
    peer_hidden, peer_scaled = from_partner((hidden_act, theirs), "dp", 0)
    own_term = lax.dot_general(
        hidden_act, own_cols, contract_rows, preferred_element_type=jnp.float32
    ).astype(jnp.bfloat16)
    peer_term = lax.dot_general(
        peer_hidden, peer_scaled, contract_rows, preferred_element_type=jnp.float32
    ).astype(jnp.bfloat16)
    own_term, peer_term = lax.optimization_barrier((own_term, peer_term))
    summed = own_term.astype(jnp.float32) + peer_term.astype(jnp.float32)
    grad_down = summed.astype(jnp.bfloat16)
    return (grad_down, grad_hidden, gate_grad)


def solution(mesh):
    in_specs = (
        P(("expert", "dp"), "tensor"),
        P(("expert", "dp"), None),
        P(("expert", "dp"), None),
        P(("expert", "dp"), None),
        P("expert", "dp", "tensor"),
        P("expert", "tensor", "dp"),
    )
    out_specs = (
        P("expert", "tensor", "dp"),
        P("expert", "dp", "tensor"),
        P(("expert", "dp"), None),
    )
    return jax.shard_map(body, mesh=mesh, in_specs=in_specs, out_specs=out_specs, check_vma=False)
```

```python
import jax
import jax.numpy as jnp
from jax import lax
from jax.sharding import PartitionSpec as P


def from_partner(value, axis, stride):
    mask = 2**stride
    pairs = [(source, source ^ mask) for source in range(lax.axis_size(axis))]
    return lax.ppermute(value, axis, pairs)


def tree_sum(value, axis):
    stride = 0
    while 2**stride < lax.axis_size(axis):
        value = value + from_partner(value, axis, stride)
        stride += 1
    return value


def body(out_grad, expert_ids, gate_weights, keep, hidden_act, down_weight):
    token_count = out_grad.shape[0]
    experts = lax.axis_size("expert")
    local_experts = hidden_act.shape[0]
    total_experts = experts * local_experts
    slot_count = hidden_act.shape[1]
    capacity = slot_count // experts
    places = total_experts * capacity
    chosen = expert_ids.reshape(-1)
    count = chosen.shape[0]
    onehot = chosen[:, None] == jnp.arange(total_experts, dtype=jnp.int32)[None, :]
    earlier = (
        jnp.arange(count, dtype=jnp.int32)[:, None] > jnp.arange(count, dtype=jnp.int32)[None, :]
    ).astype(jnp.bfloat16)
    ranking = jnp.dot(earlier, onehot.astype(jnp.bfloat16), preferred_element_type=jnp.float32)
    slot = jnp.sum(jnp.where(onehot, ranking, 0.0), axis=1).astype(jnp.int32)
    position = chosen * capacity + slot
    pos2 = position.reshape(token_count, 2)
    iota_p = jnp.arange(places, dtype=jnp.int32)[:, None]
    pick0 = pos2[None, :, 0] == iota_p
    pick1 = pos2[None, :, 1] == iota_p
    kept = keep.astype(jnp.float32)
    scale = (gate_weights * kept).astype(jnp.bfloat16)
    slot_scale = (
        jnp.dot(pick0.astype(jnp.bfloat16), scale[:, 0], preferred_element_type=jnp.float32)
        + jnp.dot(pick1.astype(jnp.bfloat16), scale[:, 1], preferred_element_type=jnp.float32)
    ).astype(jnp.bfloat16).reshape(experts, local_experts, capacity)
    arrived_scale = lax.all_to_all(slot_scale, "expert", split_axis=0, concat_axis=2, tiled=True)
    weight = arrived_scale.reshape(local_experts, slot_count).astype(jnp.float32)
    gathered = lax.all_gather(out_grad, "tensor", axis=1, tiled=True)
    full_weight = lax.all_gather(down_weight, "dp", axis=2, tiled=True)
    placing = (pick0 | pick1).astype(jnp.bfloat16).reshape(experts, local_experts, capacity, -1)
    half_width = gathered.shape[1] // 2
    dp_index = lax.axis_index("dp")
    grad_rows, scores_local, own_terms, peer_terms = [], [], [], []
    peer_hidden = from_partner(hidden_act, "dp", 0)
    for local in range(local_experts):
        outgoing = lax.dot_general(
            placing[:, local], gathered, (((2,), (0,)), ((), ())),
            preferred_element_type=jnp.float32,
        ).astype(jnp.bfloat16)
        routed = lax.all_to_all(
            outgoing, "expert", split_axis=0, concat_axis=0, tiled=True
        ).reshape(slot_count, -1)
        backprop = jnp.dot(routed, full_weight[local].T, preferred_element_type=jnp.float32)
        grad_rows.append((weight[local][:, None] * backprop).astype(jnp.bfloat16))
        scores_local.append(
            jnp.sum(backprop * hidden_act[local].astype(jnp.float32), axis=1)
        )
        scaled = (weight[local][:, None] * routed.astype(jnp.float32)).astype(jnp.bfloat16)
        own_cols = lax.dynamic_slice_in_dim(scaled, dp_index * half_width, half_width, 1)
        theirs = lax.dynamic_slice_in_dim(scaled, (1 - dp_index) * half_width, half_width, 1)
        peer_scaled = from_partner(theirs, "dp", 0)
        own_terms.append(
            jnp.dot(hidden_act[local].T, own_cols, preferred_element_type=jnp.float32).astype(
                jnp.bfloat16
            )
        )
        peer_terms.append(
            jnp.dot(peer_hidden[local].T, peer_scaled, preferred_element_type=jnp.float32).astype(
                jnp.bfloat16
            )
        )
    grad_hidden = jnp.stack(grad_rows)
    scores = tree_sum(jnp.stack(scores_local), "tensor")
    returned = lax.all_to_all(
        scores.reshape(local_experts, experts, capacity),
        "expert",
        split_axis=1,
        concat_axis=0,
        tiled=True,
    ).reshape(-1)
    picked = jnp.sum(
        jnp.where(position[:, None] == iota_p[None, :, 0], returned[None, :], 0.0), axis=1
    )
    gate_grad = picked.reshape(token_count, 2) * kept
    own_term, peer_term = lax.optimization_barrier((jnp.stack(own_terms), jnp.stack(peer_terms)))
    summed = own_term.astype(jnp.float32) + peer_term.astype(jnp.float32)
    grad_down = summed.astype(jnp.bfloat16)
    return (grad_down, grad_hidden, gate_grad)


def solution(mesh):
    in_specs = (
        P(("expert", "dp"), "tensor"),
        P(("expert", "dp"), None),
        P(("expert", "dp"), None),
        P(("expert", "dp"), None),
        P("expert", "dp", "tensor"),
        P("expert", "tensor", "dp"),
    )
    out_specs = (
        P("expert", "tensor", "dp"),
        P("expert", "dp", "tensor"),
        P(("expert", "dp"), None),
    )
    return jax.shard_map(body, mesh=mesh, in_specs=in_specs, out_specs=out_specs, check_vma=False)
```

```python
import jax
import jax.numpy as jnp
from jax import lax
from jax.sharding import PartitionSpec as P


def from_partner(value, axis, stride):
    mask = 2**stride
    pairs = [(source, source ^ mask) for source in range(lax.axis_size(axis))]
    return lax.ppermute(value, axis, pairs)


def tree_sum(value, axis):
    stride = 0
    while 2**stride < lax.axis_size(axis):
        value = value + from_partner(value, axis, stride)
        stride += 1
    return value


def body(out_grad, expert_ids, gate_weights, keep, hidden_act, down_weight):
    token_count, width = out_grad.shape
    tensor_size = lax.axis_size("tensor")
    experts = lax.axis_size("expert")
    local_experts = hidden_act.shape[0]
    hidden = hidden_act.shape[2]
    total_experts = experts * local_experts
    slot_count = hidden_act.shape[1]
    capacity = slot_count // experts
    places = total_experts * capacity
    split = width // 2
    chosen = expert_ids.reshape(-1)
    count = chosen.shape[0]
    onehot = chosen[:, None] == jnp.arange(total_experts, dtype=jnp.int32)[None, :]
    earlier = (
        jnp.arange(count, dtype=jnp.int32)[:, None] > jnp.arange(count, dtype=jnp.int32)[None, :]
    ).astype(jnp.bfloat16)
    ranking = jnp.dot(earlier, onehot.astype(jnp.bfloat16), preferred_element_type=jnp.float32)
    slot = jnp.sum(jnp.where(onehot, ranking, 0.0), axis=1).astype(jnp.int32)
    position = chosen * capacity + slot
    pos2 = position.reshape(token_count, 2)
    iota_p = jnp.arange(places, dtype=jnp.int32)[:, None]
    pick0 = pos2[None, :, 0] == iota_p
    pick1 = pos2[None, :, 1] == iota_p
    kept = keep.astype(jnp.float32)
    scale = (gate_weights * kept).astype(jnp.bfloat16)
    slot_scale = (
        jnp.dot(pick0.astype(jnp.bfloat16), scale[:, 0], preferred_element_type=jnp.float32)
        + jnp.dot(pick1.astype(jnp.bfloat16), scale[:, 1], preferred_element_type=jnp.float32)
    ).astype(jnp.bfloat16).reshape(experts, local_experts, capacity)
    placing = (pick0 | pick1).astype(jnp.bfloat16).reshape(experts, local_experts, capacity, -1)

    outgoing_b = lax.dot_general(
        placing, out_grad[:, split:], (((3,), (0,)), ((), ())),
        preferred_element_type=jnp.float32,
    ).astype(jnp.bfloat16)
    arrived_b, arrived_scale = (
        lax.all_to_all(outgoing_b, "expert", split_axis=0, concat_axis=2, tiled=True),
        lax.all_to_all(slot_scale, "expert", split_axis=0, concat_axis=2, tiled=True),
    )
    weight = arrived_scale.reshape(local_experts, slot_count).astype(jnp.float32)
    routed_b = lax.all_gather(
        arrived_b.reshape(local_experts, slot_count, split), "tensor", axis=2, tiled=True
    )

    gathered_a = lax.all_gather(out_grad[:, :split], "tensor", axis=1, tiled=True)

    dp_index = lax.axis_index("dp")
    partner_weight = from_partner(down_weight, "dp", 0)
    first = jnp.where(dp_index == 0, down_weight, partner_weight)
    second = jnp.where(dp_index == 0, partner_weight, down_weight)
    halves = tensor_size // 2
    full_weight = jnp.concatenate([first, second], axis=2).reshape(
        local_experts, hidden, tensor_size, 2, split
    )
    weight_a = full_weight[:, :, :, 0, :].reshape(local_experts, hidden, tensor_size * split)
    weight_b = full_weight[:, :, :, 1, :].reshape(local_experts, hidden, tensor_size * split)

    peer_hidden = from_partner(hidden_act, "dp", 0)
    own_start = dp_index * halves * split
    peer_start = (1 - dp_index) * halves * split
    own_width = halves * split

    scaled_b = (weight[:, :, None] * routed_b.astype(jnp.float32)).astype(jnp.bfloat16)
    own_b = lax.dynamic_slice_in_dim(scaled_b, own_start, own_width, 2)
    peer_b = from_partner(lax.dynamic_slice_in_dim(scaled_b, peer_start, own_width, 2), "dp", 0)

    grad_rows, scores_local, own_terms, peer_terms = [], [], [], []
    for local in range(local_experts):
        outgoing_a = lax.dot_general(
            placing[:, local], gathered_a, (((2,), (0,)), ((), ())),
            preferred_element_type=jnp.float32,
        ).astype(jnp.bfloat16)
        routed_a = lax.all_to_all(
            outgoing_a, "expert", split_axis=0, concat_axis=0, tiled=True
        ).reshape(slot_count, -1)
        backprop = jnp.dot(
            routed_a, weight_a[local].T, preferred_element_type=jnp.float32
        ) + jnp.dot(routed_b[local], weight_b[local].T, preferred_element_type=jnp.float32)
        grad_rows.append((weight[local][:, None] * backprop).astype(jnp.bfloat16))
        scores_local.append(
            jnp.sum(backprop * hidden_act[local].astype(jnp.float32), axis=1)
        )
        scaled_a = (weight[local][:, None] * routed_a.astype(jnp.float32)).astype(jnp.bfloat16)
        own_a = lax.dynamic_slice_in_dim(scaled_a, own_start, own_width, 1)
        peer_a = from_partner(
            lax.dynamic_slice_in_dim(scaled_a, peer_start, own_width, 1), "dp", 0
        )
        own_terms.append(
            jnp.stack(
                [
                    jnp.dot(hidden_act[local].T, own_a, preferred_element_type=jnp.float32),
                    jnp.dot(hidden_act[local].T, own_b[local], preferred_element_type=jnp.float32),
                ],
                axis=0,
            ).astype(jnp.bfloat16)
        )
        peer_terms.append(
            jnp.stack(
                [
                    jnp.dot(peer_hidden[local].T, peer_a, preferred_element_type=jnp.float32),
                    jnp.dot(
                        peer_hidden[local].T, peer_b[local], preferred_element_type=jnp.float32
                    ),
                ],
                axis=0,
            ).astype(jnp.bfloat16)
        )
    grad_hidden = jnp.stack(grad_rows)
    scores = tree_sum(jnp.stack(scores_local), "tensor")
    returned = lax.all_to_all(
        scores.reshape(local_experts, experts, capacity),
        "expert",
        split_axis=1,
        concat_axis=0,
        tiled=True,
    ).reshape(-1)
    picked = jnp.sum(
        jnp.where(position[:, None] == iota_p[None, :, 0], returned[None, :], 0.0), axis=1
    )
    gate_grad = picked.reshape(token_count, 2) * kept
    own_term, peer_term = lax.optimization_barrier((jnp.stack(own_terms), jnp.stack(peer_terms)))
    summed = own_term.astype(jnp.float32) + peer_term.astype(jnp.float32)
    summed = summed.reshape(local_experts, 2, hidden, halves, split).transpose(0, 2, 3, 1, 4)
    grad_down = summed.reshape(local_experts, hidden, 2 * halves * split).astype(jnp.bfloat16)
    return (grad_down, grad_hidden, gate_grad)


def solution(mesh):
    in_specs = (
        P(("expert", "dp"), "tensor"),
        P(("expert", "dp"), None),
        P(("expert", "dp"), None),
        P(("expert", "dp"), None),
        P("expert", "dp", "tensor"),
        P("expert", "tensor", "dp"),
    )
    out_specs = (
        P("expert", "tensor", "dp"),
        P("expert", "dp", "tensor"),
        P(("expert", "dp"), None),
    )
    return jax.shard_map(body, mesh=mesh, in_specs=in_specs, out_specs=out_specs, check_vma=False)
```

```python
import jax
import jax.numpy as jnp
from jax import lax
from jax.sharding import PartitionSpec as P


def from_partner(value, axis, stride):
    mask = 2**stride
    pairs = [(source, source ^ mask) for source in range(lax.axis_size(axis))]
    return lax.ppermute(value, axis, pairs)


def tree_sum(value, axis):
    stride = 0
    while 2**stride < lax.axis_size(axis):
        value = value + from_partner(value, axis, stride)
        stride += 1
    return value


def ring_gather(value, axis):
    size = lax.axis_size(axis)
    index = lax.axis_index(axis)
    right = [(source, (source + 1) % size) for source in range(size)]
    left = [(source, (source - 1) % size) for source in range(size)]
    gathered = jnp.zeros((size,) + value.shape, value.dtype)
    gathered = lax.dynamic_update_index_in_dim(gathered, value, index, 0)
    going_right = going_left = value
    for step in range(1, size // 2 + 1):
        going_right = lax.ppermute(going_right, axis, right)
        gathered = lax.dynamic_update_index_in_dim(
            gathered, going_right, (index + size - step) % size, 0
        )
        if step < size - size // 2:
            going_left = lax.ppermute(going_left, axis, left)
            gathered = lax.dynamic_update_index_in_dim(
                gathered, going_left, (index + step) % size, 0
            )
    return gathered

def body(out_grad, expert_ids, gate_weights, keep, hidden_act, down_weight):
    token_count = out_grad.shape[0]
    experts = lax.axis_size("expert")
    local_experts = hidden_act.shape[0]
    total_experts = experts * local_experts
    slot_count = hidden_act.shape[1]
    capacity = slot_count // experts
    places = total_experts * capacity
    chosen = expert_ids.reshape(-1)
    count = chosen.shape[0]
    onehot = chosen[:, None] == jnp.arange(total_experts, dtype=jnp.int32)[None, :]
    earlier = (
        jnp.arange(count, dtype=jnp.int32)[:, None] > jnp.arange(count, dtype=jnp.int32)[None, :]
    ).astype(jnp.bfloat16)
    ranking = jnp.dot(earlier, onehot.astype(jnp.bfloat16), preferred_element_type=jnp.float32)
    slot = jnp.sum(jnp.where(onehot, ranking, 0.0), axis=1).astype(jnp.int32)
    position = chosen * capacity + slot
    pos2 = position.reshape(token_count, 2)
    iota_p = jnp.arange(places, dtype=jnp.int32)[:, None]
    pick0 = pos2[None, :, 0] == iota_p
    pick1 = pos2[None, :, 1] == iota_p
    kept = keep.astype(jnp.float32)
    scale = (gate_weights * kept).astype(jnp.bfloat16)
    slot_scale = (
        jnp.dot(pick0.astype(jnp.bfloat16), scale[:, 0], preferred_element_type=jnp.float32)
        + jnp.dot(pick1.astype(jnp.bfloat16), scale[:, 1], preferred_element_type=jnp.float32)
    ).astype(jnp.bfloat16).reshape(experts, local_experts, capacity)
    arrived_scale = lax.all_to_all(slot_scale, "expert", split_axis=0, concat_axis=2, tiled=True)
    weight = arrived_scale.reshape(local_experts, slot_count).astype(jnp.float32)
    gathered = ring_gather(out_grad, "tensor")
    full_weight = lax.all_gather(down_weight, "dp", axis=2, tiled=True)
    placing = (pick0 | pick1).astype(jnp.bfloat16).reshape(experts, local_experts, capacity, -1)
    half_width = gathered.shape[0] * gathered.shape[2] // 2
    dp_index = lax.axis_index("dp")
    grad_rows, scores_local, own_terms, peer_terms = [], [], [], []
    peer_hidden = from_partner(hidden_act, "dp", 0)
    for local in range(local_experts):
        outgoing = lax.dot_general(
            placing[:, local], gathered, (((2,), (1,)), ((), ())),
            preferred_element_type=jnp.float32,
        ).astype(jnp.bfloat16).reshape(experts, capacity, -1)
        routed = lax.all_to_all(
            outgoing, "expert", split_axis=0, concat_axis=0, tiled=True
        ).reshape(slot_count, -1)
        backprop = jnp.dot(routed, full_weight[local].T, preferred_element_type=jnp.float32)
        grad_rows.append((weight[local][:, None] * backprop).astype(jnp.bfloat16))
        scores_local.append(
            jnp.sum(backprop * hidden_act[local].astype(jnp.float32), axis=1)
        )
        scaled = (weight[local][:, None] * routed.astype(jnp.float32)).astype(jnp.bfloat16)
        own_cols = lax.dynamic_slice_in_dim(scaled, dp_index * half_width, half_width, 1)
        theirs = lax.dynamic_slice_in_dim(scaled, (1 - dp_index) * half_width, half_width, 1)
        peer_scaled = from_partner(theirs, "dp", 0)
        own_terms.append(
            jnp.dot(hidden_act[local].T, own_cols, preferred_element_type=jnp.float32).astype(
                jnp.bfloat16
            )
        )
        peer_terms.append(
            jnp.dot(peer_hidden[local].T, peer_scaled, preferred_element_type=jnp.float32).astype(
                jnp.bfloat16
            )
        )
    grad_hidden = jnp.stack(grad_rows)
    scores = tree_sum(jnp.stack(scores_local), "tensor")
    returned = lax.all_to_all(
        scores.reshape(local_experts, experts, capacity),
        "expert",
        split_axis=1,
        concat_axis=0,
        tiled=True,
    ).reshape(-1)
    picked = jnp.sum(
        jnp.where(position[:, None] == iota_p[None, :, 0], returned[None, :], 0.0), axis=1
    )
    gate_grad = picked.reshape(token_count, 2) * kept
    own_term, peer_term = lax.optimization_barrier((jnp.stack(own_terms), jnp.stack(peer_terms)))
    summed = own_term.astype(jnp.float32) + peer_term.astype(jnp.float32)
    grad_down = summed.astype(jnp.bfloat16)
    return (grad_down, grad_hidden, gate_grad)


def solution(mesh):
    in_specs = (
        P(("expert", "dp"), "tensor"),
        P(("expert", "dp"), None),
        P(("expert", "dp"), None),
        P(("expert", "dp"), None),
        P("expert", "dp", "tensor"),
        P("expert", "tensor", "dp"),
    )
    out_specs = (
        P("expert", "tensor", "dp"),
        P("expert", "dp", "tensor"),
        P(("expert", "dp"), None),
    )
    return jax.shard_map(body, mesh=mesh, in_specs=in_specs, out_specs=out_specs, check_vma=False)
```

```python
import jax
import jax.numpy as jnp
from jax import lax
from jax.sharding import PartitionSpec as P


def from_partner(value, axis, stride):
    mask = 2**stride
    pairs = [(source, source ^ mask) for source in range(lax.axis_size(axis))]
    return lax.ppermute(value, axis, pairs)


def tree_sum(value, axis):
    stride = 0
    while 2**stride < lax.axis_size(axis):
        value = value + from_partner(value, axis, stride)
        stride += 1
    return value


def ring_gather(value, axis):
    size = lax.axis_size(axis)
    index = lax.axis_index(axis)
    right = [(source, (source + 1) % size) for source in range(size)]
    left = [(source, (source - 1) % size) for source in range(size)]
    width = value.shape[1]
    gathered = jnp.zeros((value.shape[0], size * width), value.dtype)
    gathered = lax.dynamic_update_slice_in_dim(gathered, value, index * width, 1)
    going_right = going_left = value
    for step in range(1, size // 2 + 1):
        going_right = lax.ppermute(going_right, axis, right)
        gathered = lax.dynamic_update_slice_in_dim(
            gathered, going_right, (index + size - step) % size * width, 1
        )
        if step < size - size // 2:
            going_left = lax.ppermute(going_left, axis, left)
            gathered = lax.dynamic_update_slice_in_dim(
                gathered, going_left, (index + step) % size * width, 1
            )
    return gathered

def body(out_grad, expert_ids, gate_weights, keep, hidden_act, down_weight):
    token_count = out_grad.shape[0]
    experts = lax.axis_size("expert")
    local_experts = hidden_act.shape[0]
    total_experts = experts * local_experts
    slot_count = hidden_act.shape[1]
    capacity = slot_count // experts
    places = total_experts * capacity
    chosen = expert_ids.reshape(-1)
    count = chosen.shape[0]
    onehot = chosen[:, None] == jnp.arange(total_experts, dtype=jnp.int32)[None, :]
    earlier = (
        jnp.arange(count, dtype=jnp.int32)[:, None] > jnp.arange(count, dtype=jnp.int32)[None, :]
    ).astype(jnp.bfloat16)
    ranking = jnp.dot(earlier, onehot.astype(jnp.bfloat16), preferred_element_type=jnp.float32)
    slot = jnp.sum(jnp.where(onehot, ranking, 0.0), axis=1).astype(jnp.int32)
    position = chosen * capacity + slot
    pos2 = position.reshape(token_count, 2)
    iota_p = jnp.arange(places, dtype=jnp.int32)[:, None]
    pick0 = pos2[None, :, 0] == iota_p
    pick1 = pos2[None, :, 1] == iota_p
    kept = keep.astype(jnp.float32)
    scale = (gate_weights * kept).astype(jnp.bfloat16)
    slot_scale = (
        jnp.dot(pick0.astype(jnp.bfloat16), scale[:, 0], preferred_element_type=jnp.float32)
        + jnp.dot(pick1.astype(jnp.bfloat16), scale[:, 1], preferred_element_type=jnp.float32)
    ).astype(jnp.bfloat16).reshape(experts, local_experts, capacity)
    arrived_scale = lax.all_to_all(slot_scale, "expert", split_axis=0, concat_axis=2, tiled=True)
    weight = arrived_scale.reshape(local_experts, slot_count).astype(jnp.float32)
    gathered = ring_gather(out_grad, "tensor")
    full_weight = lax.all_gather(down_weight, "dp", axis=2, tiled=True)
    placing = (pick0 | pick1).astype(jnp.bfloat16).reshape(experts, local_experts, capacity, -1)
    half_width = gathered.shape[1] // 2
    dp_index = lax.axis_index("dp")
    grad_rows, scores_local, own_terms, peer_terms = [], [], [], []
    peer_hidden = from_partner(hidden_act, "dp", 0)
    outgoing = lax.dot_general(
        placing.reshape(experts, local_experts * capacity, -1), gathered,
        (((2,), (0,)), ((), ())),
        preferred_element_type=jnp.float32,
    ).astype(jnp.bfloat16)
    arrived = lax.all_to_all(outgoing, "expert", split_axis=0, concat_axis=0, tiled=True)
    routed_all = arrived.reshape(experts, local_experts, capacity, -1).transpose(1, 0, 2, 3)
    routed_all = routed_all.reshape(local_experts, slot_count, -1)
    for local in range(local_experts):
        routed = routed_all[local]
        backprop = jnp.dot(routed, full_weight[local].T, preferred_element_type=jnp.float32)
        grad_rows.append((weight[local][:, None] * backprop).astype(jnp.bfloat16))
        scores_local.append(
            jnp.sum(backprop * hidden_act[local].astype(jnp.float32), axis=1)
        )
        scaled = (weight[local][:, None] * routed.astype(jnp.float32)).astype(jnp.bfloat16)
        own_cols = lax.dynamic_slice_in_dim(scaled, dp_index * half_width, half_width, 1)
        theirs = lax.dynamic_slice_in_dim(scaled, (1 - dp_index) * half_width, half_width, 1)
        peer_scaled = from_partner(theirs, "dp", 0)
        own_terms.append(
            jnp.dot(hidden_act[local].T, own_cols, preferred_element_type=jnp.float32).astype(
                jnp.bfloat16
            )
        )
        peer_terms.append(
            jnp.dot(peer_hidden[local].T, peer_scaled, preferred_element_type=jnp.float32).astype(
                jnp.bfloat16
            )
        )
    grad_hidden = jnp.stack(grad_rows)
    scores = tree_sum(jnp.stack(scores_local), "tensor")
    returned = lax.all_to_all(
        scores.reshape(local_experts, experts, capacity),
        "expert",
        split_axis=1,
        concat_axis=0,
        tiled=True,
    ).reshape(-1)
    picked = jnp.sum(
        jnp.where(position[:, None] == iota_p[None, :, 0], returned[None, :], 0.0), axis=1
    )
    gate_grad = picked.reshape(token_count, 2) * kept
    own_term, peer_term = lax.optimization_barrier((jnp.stack(own_terms), jnp.stack(peer_terms)))
    summed = own_term.astype(jnp.float32) + peer_term.astype(jnp.float32)
    grad_down = summed.astype(jnp.bfloat16)
    return (grad_down, grad_hidden, gate_grad)


def solution(mesh):
    in_specs = (
        P(("expert", "dp"), "tensor"),
        P(("expert", "dp"), None),
        P(("expert", "dp"), None),
        P(("expert", "dp"), None),
        P("expert", "dp", "tensor"),
        P("expert", "tensor", "dp"),
    )
    out_specs = (
        P("expert", "tensor", "dp"),
        P("expert", "dp", "tensor"),
        P(("expert", "dp"), None),
    )
    return jax.shard_map(body, mesh=mesh, in_specs=in_specs, out_specs=out_specs, check_vma=False)
```

```python
import jax
import jax.numpy as jnp
from jax import lax
from jax.sharding import PartitionSpec as P


def from_partner(value, axis, stride):
    mask = 2**stride
    pairs = [(source, source ^ mask) for source in range(lax.axis_size(axis))]
    return lax.ppermute(value, axis, pairs)


def tree_sum(value, axis):
    stride = 0
    while 2**stride < lax.axis_size(axis):
        value = value + from_partner(value, axis, stride)
        stride += 1
    return value


def ring_gather(value, axis):
    size = lax.axis_size(axis)
    index = lax.axis_index(axis)
    right = [(source, (source + 1) % size) for source in range(size)]
    left = [(source, (source - 1) % size) for source in range(size)]
    width = value.shape[1]
    gathered = jnp.zeros((value.shape[0], size * width), value.dtype)
    gathered = lax.dynamic_update_slice_in_dim(gathered, value, index * width, 1)
    going_right = going_left = value
    for step in range(1, size // 2 + 1):
        going_right = lax.ppermute(going_right, axis, right)
        gathered = lax.dynamic_update_slice_in_dim(
            gathered, going_right, (index + size - step) % size * width, 1
        )
        if step < size - size // 2:
            going_left = lax.ppermute(going_left, axis, left)
            gathered = lax.dynamic_update_slice_in_dim(
                gathered, going_left, (index + step) % size * width, 1
            )
    return gathered

def body(out_grad, expert_ids, gate_weights, keep, hidden_act, down_weight):
    token_count = out_grad.shape[0]
    experts = lax.axis_size("expert")
    local_experts = hidden_act.shape[0]
    total_experts = experts * local_experts
    slot_count = hidden_act.shape[1]
    capacity = slot_count // experts
    places = total_experts * capacity
    chosen = expert_ids.reshape(-1)
    count = chosen.shape[0]
    onehot = chosen[:, None] == jnp.arange(total_experts, dtype=jnp.int32)[None, :]
    earlier = (
        jnp.arange(count, dtype=jnp.int32)[:, None] > jnp.arange(count, dtype=jnp.int32)[None, :]
    ).astype(jnp.bfloat16)
    ranking = jnp.dot(earlier, onehot.astype(jnp.bfloat16), preferred_element_type=jnp.float32)
    slot = jnp.sum(jnp.where(onehot, ranking, 0.0), axis=1).astype(jnp.int32)
    position = chosen * capacity + slot
    pos2 = position.reshape(token_count, 2)
    iota_p = jnp.arange(places, dtype=jnp.int32)[:, None]
    pick0 = pos2[None, :, 0] == iota_p
    pick1 = pos2[None, :, 1] == iota_p
    kept = keep.astype(jnp.float32)
    scale = (gate_weights * kept).astype(jnp.bfloat16)
    slot_scale = (
        jnp.dot(pick0.astype(jnp.bfloat16), scale[:, 0], preferred_element_type=jnp.float32)
        + jnp.dot(pick1.astype(jnp.bfloat16), scale[:, 1], preferred_element_type=jnp.float32)
    ).astype(jnp.bfloat16).reshape(experts, local_experts, capacity)
    arrived_scale = lax.all_to_all(slot_scale, "expert", split_axis=0, concat_axis=2, tiled=True)
    weight = arrived_scale.reshape(local_experts, slot_count).astype(jnp.float32)
    width = out_grad.shape[1]
    split = width // 2
    tensor_size = lax.axis_size("tensor")
    full_weight = lax.all_gather(down_weight, "dp", axis=2, tiled=True)
    placing = (pick0 | pick1).astype(jnp.bfloat16).reshape(experts, local_experts * capacity, -1)
    dp_index = lax.axis_index("dp")
    grad_rows, scores_local, own_terms, peer_terms = [], [], [], []
    peer_hidden = from_partner(hidden_act, "dp", 0)

    def to_experts(columns):
        outgoing = lax.dot_general(
            placing, columns, (((2,), (0,)), ((), ())), preferred_element_type=jnp.float32
        ).astype(jnp.bfloat16)
        arrived = lax.all_to_all(outgoing, "expert", split_axis=0, concat_axis=0, tiled=True)
        return arrived.reshape(experts, local_experts, capacity, -1).transpose(1, 0, 2, 3)

    arrived_b = to_experts(out_grad[:, split:]).reshape(local_experts * slot_count, split)
    routed_b = ring_gather(arrived_b, "tensor").reshape(local_experts, slot_count, tensor_size, split)
    gathered_a = ring_gather(out_grad[:, :split], "tensor")
    routed_a = to_experts(gathered_a).reshape(local_experts, slot_count, tensor_size, split)
    routed_all = jnp.stack([routed_a, routed_b], axis=3).reshape(local_experts, slot_count, -1)
    half_width = routed_all.shape[2] // 2
    for local in range(local_experts):
        routed = routed_all[local]
        backprop = jnp.dot(routed, full_weight[local].T, preferred_element_type=jnp.float32)
        grad_rows.append((weight[local][:, None] * backprop).astype(jnp.bfloat16))
        scores_local.append(
            jnp.sum(backprop * hidden_act[local].astype(jnp.float32), axis=1)
        )
        scaled = (weight[local][:, None] * routed.astype(jnp.float32)).astype(jnp.bfloat16)
        own_cols = lax.dynamic_slice_in_dim(scaled, dp_index * half_width, half_width, 1)
        theirs = lax.dynamic_slice_in_dim(scaled, (1 - dp_index) * half_width, half_width, 1)
        peer_scaled = from_partner(theirs, "dp", 0)
        own_terms.append(
            jnp.dot(hidden_act[local].T, own_cols, preferred_element_type=jnp.float32).astype(
                jnp.bfloat16
            )
        )
        peer_terms.append(
            jnp.dot(peer_hidden[local].T, peer_scaled, preferred_element_type=jnp.float32).astype(
                jnp.bfloat16
            )
        )
    grad_hidden = jnp.stack(grad_rows)
    scores = tree_sum(jnp.stack(scores_local), "tensor")
    returned = lax.all_to_all(
        scores.reshape(local_experts, experts, capacity),
        "expert",
        split_axis=1,
        concat_axis=0,
        tiled=True,
    ).reshape(-1)
    picked = jnp.sum(
        jnp.where(position[:, None] == iota_p[None, :, 0], returned[None, :], 0.0), axis=1
    )
    gate_grad = picked.reshape(token_count, 2) * kept
    own_term, peer_term = lax.optimization_barrier((jnp.stack(own_terms), jnp.stack(peer_terms)))
    summed = own_term.astype(jnp.float32) + peer_term.astype(jnp.float32)
    grad_down = summed.astype(jnp.bfloat16)
    return (grad_down, grad_hidden, gate_grad)


def solution(mesh):
    in_specs = (
        P(("expert", "dp"), "tensor"),
        P(("expert", "dp"), None),
        P(("expert", "dp"), None),
        P(("expert", "dp"), None),
        P("expert", "dp", "tensor"),
        P("expert", "tensor", "dp"),
    )
    out_specs = (
        P("expert", "tensor", "dp"),
        P("expert", "dp", "tensor"),
        P(("expert", "dp"), None),
    )
    return jax.shard_map(body, mesh=mesh, in_specs=in_specs, out_specs=out_specs, check_vma=False)
```

```python
import jax
import jax.numpy as jnp
from jax import lax
from jax.sharding import PartitionSpec as P


def from_partner(value, axis, stride):
    mask = 2**stride
    pairs = [(source, source ^ mask) for source in range(lax.axis_size(axis))]
    return lax.ppermute(value, axis, pairs)


def tree_sum(value, axis):
    stride = 0
    while 2**stride < lax.axis_size(axis):
        value = value + from_partner(value, axis, stride)
        stride += 1
    return value


def ring_gather(value, axis):
    size = lax.axis_size(axis)
    index = lax.axis_index(axis)
    right = [(source, (source + 1) % size) for source in range(size)]
    left = [(source, (source - 1) % size) for source in range(size)]
    width = value.shape[1]
    gathered = jnp.zeros((value.shape[0], size * width), value.dtype)
    gathered = lax.dynamic_update_slice_in_dim(gathered, value, index * width, 1)
    going_right = going_left = value
    for step in range(1, size // 2 + 1):
        going_right = lax.ppermute(going_right, axis, right)
        gathered = lax.dynamic_update_slice_in_dim(
            gathered, going_right, (index + size - step) % size * width, 1
        )
        if step < size - size // 2:
            going_left = lax.ppermute(going_left, axis, left)
            gathered = lax.dynamic_update_slice_in_dim(
                gathered, going_left, (index + step) % size * width, 1
            )
    return gathered

def body(out_grad, expert_ids, gate_weights, keep, hidden_act, down_weight):
    token_count = out_grad.shape[0]
    experts = lax.axis_size("expert")
    local_experts = hidden_act.shape[0]
    total_experts = experts * local_experts
    slot_count = hidden_act.shape[1]
    capacity = slot_count // experts
    places = total_experts * capacity
    chosen = expert_ids.reshape(-1)
    count = chosen.shape[0]
    onehot = chosen[:, None] == jnp.arange(total_experts, dtype=jnp.int32)[None, :]
    earlier = (
        jnp.arange(count, dtype=jnp.int32)[:, None] > jnp.arange(count, dtype=jnp.int32)[None, :]
    ).astype(jnp.bfloat16)
    ranking = jnp.dot(earlier, onehot.astype(jnp.bfloat16), preferred_element_type=jnp.float32)
    slot = jnp.sum(jnp.where(onehot, ranking, 0.0), axis=1).astype(jnp.int32)
    position = chosen * capacity + slot
    pos2 = position.reshape(token_count, 2)
    iota_p = jnp.arange(places, dtype=jnp.int32)[:, None]
    pick0 = pos2[None, :, 0] == iota_p
    pick1 = pos2[None, :, 1] == iota_p
    kept = keep.astype(jnp.float32)
    scale = (gate_weights * kept).astype(jnp.bfloat16)
    slot_scale = (
        jnp.dot(pick0.astype(jnp.bfloat16), scale[:, 0], preferred_element_type=jnp.float32)
        + jnp.dot(pick1.astype(jnp.bfloat16), scale[:, 1], preferred_element_type=jnp.float32)
    ).astype(jnp.bfloat16).reshape(experts, local_experts, capacity)
    arrived_scale = lax.all_to_all(slot_scale, "expert", split_axis=0, concat_axis=2, tiled=True)
    weight = arrived_scale.reshape(local_experts, slot_count).astype(jnp.float32)
    width = out_grad.shape[1]
    split = width // 2
    tensor_size = lax.axis_size("tensor")
    full_weight = lax.all_gather(down_weight, "dp", axis=2, tiled=True)
    placing = (pick0 | pick1).astype(jnp.bfloat16).reshape(experts, local_experts * capacity, -1)
    dp_index = lax.axis_index("dp")
    grad_rows, scores_local, own_terms, peer_terms = [], [], [], []
    peer_hidden = from_partner(hidden_act, "dp", 0)

    def to_experts(columns, rows):
        outgoing = lax.dot_general(
            rows, columns, (((2,), (0,)), ((), ())), preferred_element_type=jnp.float32
        ).astype(jnp.bfloat16)
        return lax.all_to_all(outgoing, "expert", split_axis=0, concat_axis=0, tiled=True)

    sets = full_weight.reshape(local_experts, -1, tensor_size, 2, split)
    weight_a = sets[:, :, :, 0, :].reshape(local_experts, -1, tensor_size * split)
    weight_b = sets[:, :, :, 1, :].reshape(local_experts, -1, tensor_size * split)

    arrived_b = to_experts(out_grad[:, split:], placing)
    arrived_b = arrived_b.reshape(experts, local_experts, capacity, split).transpose(1, 0, 2, 3)
    routed_b = ring_gather(arrived_b.reshape(local_experts * slot_count, split), "tensor")
    routed_b = routed_b.reshape(local_experts, slot_count, tensor_size * split)
    gathered_a = ring_gather(out_grad[:, :split], "tensor")
    by_expert = placing.reshape(experts, local_experts, capacity, -1)
    halves = tensor_size // 2

    for local in range(local_experts):
        routed_a = to_experts(gathered_a, by_expert[:, local]).reshape(slot_count, -1)
        backprop = jnp.dot(
            routed_a, weight_a[local].T, preferred_element_type=jnp.float32
        ) + jnp.dot(routed_b[local], weight_b[local].T, preferred_element_type=jnp.float32)
        grad_rows.append((weight[local][:, None] * backprop).astype(jnp.bfloat16))
        scores_local.append(
            jnp.sum(backprop * hidden_act[local].astype(jnp.float32), axis=1)
        )
        both = jnp.stack(
            [
                routed_a.reshape(slot_count, tensor_size, split),
                routed_b[local].reshape(slot_count, tensor_size, split),
            ],
            axis=2,
        ).reshape(slot_count, tensor_size, 2 * split)
        scaled = (weight[local][:, None, None] * both.astype(jnp.float32)).astype(jnp.bfloat16)
        own_cols = lax.dynamic_slice_in_dim(scaled, dp_index * halves, halves, 1)
        theirs = lax.dynamic_slice_in_dim(scaled, (1 - dp_index) * halves, halves, 1)
        own_cols = own_cols.reshape(slot_count, -1)
        peer_scaled = from_partner(theirs.reshape(slot_count, -1), "dp", 0)
        own_terms.append(
            jnp.dot(hidden_act[local].T, own_cols, preferred_element_type=jnp.float32).astype(
                jnp.bfloat16
            )
        )
        peer_terms.append(
            jnp.dot(peer_hidden[local].T, peer_scaled, preferred_element_type=jnp.float32).astype(
                jnp.bfloat16
            )
        )
    grad_hidden = jnp.stack(grad_rows)
    scores = tree_sum(jnp.stack(scores_local), "tensor")
    returned = lax.all_to_all(
        scores.reshape(local_experts, experts, capacity),
        "expert",
        split_axis=1,
        concat_axis=0,
        tiled=True,
    ).reshape(-1)
    picked = jnp.sum(
        jnp.where(position[:, None] == iota_p[None, :, 0], returned[None, :], 0.0), axis=1
    )
    gate_grad = picked.reshape(token_count, 2) * kept
    own_term, peer_term = lax.optimization_barrier((jnp.stack(own_terms), jnp.stack(peer_terms)))
    summed = own_term.astype(jnp.float32) + peer_term.astype(jnp.float32)
    grad_down = summed.astype(jnp.bfloat16)
    return (grad_down, grad_hidden, gate_grad)


def solution(mesh):
    in_specs = (
        P(("expert", "dp"), "tensor"),
        P(("expert", "dp"), None),
        P(("expert", "dp"), None),
        P(("expert", "dp"), None),
        P("expert", "dp", "tensor"),
        P("expert", "tensor", "dp"),
    )
    out_specs = (
        P("expert", "tensor", "dp"),
        P("expert", "dp", "tensor"),
        P(("expert", "dp"), None),
    )
    return jax.shard_map(body, mesh=mesh, in_specs=in_specs, out_specs=out_specs, check_vma=False)
```

```python
import jax
import jax.numpy as jnp
from jax import lax
from jax.sharding import PartitionSpec as P


def from_partner(value, axis, stride):
    mask = 2**stride
    pairs = [(source, source ^ mask) for source in range(lax.axis_size(axis))]
    return lax.ppermute(value, axis, pairs)


def tree_sum(value, axis):
    stride = 0
    while 2**stride < lax.axis_size(axis):
        value = value + from_partner(value, axis, stride)
        stride += 1
    return value


def ring_gather(value, axis):
    size = lax.axis_size(axis)
    index = lax.axis_index(axis)
    right = [(source, (source + 1) % size) for source in range(size)]
    left = [(source, (source - 1) % size) for source in range(size)]
    width = value.shape[1]
    gathered = jnp.zeros((value.shape[0], size * width), value.dtype)
    gathered = lax.dynamic_update_slice_in_dim(gathered, value, index * width, 1)
    going_right = going_left = value
    for step in range(1, size // 2 + 1):
        going_right = lax.ppermute(going_right, axis, right)
        gathered = lax.dynamic_update_slice_in_dim(
            gathered, going_right, (index + size - step) % size * width, 1
        )
        if step < size - size // 2:
            going_left = lax.ppermute(going_left, axis, left)
            gathered = lax.dynamic_update_slice_in_dim(
                gathered, going_left, (index + step) % size * width, 1
            )
    return gathered

def body(out_grad, expert_ids, gate_weights, keep, hidden_act, down_weight):
    token_count = out_grad.shape[0]
    experts = lax.axis_size("expert")
    local_experts = hidden_act.shape[0]
    total_experts = experts * local_experts
    slot_count = hidden_act.shape[1]
    capacity = slot_count // experts
    places = total_experts * capacity
    chosen = expert_ids.reshape(-1)
    count = chosen.shape[0]
    onehot = chosen[:, None] == jnp.arange(total_experts, dtype=jnp.int32)[None, :]
    earlier = (
        jnp.arange(count, dtype=jnp.int32)[:, None] > jnp.arange(count, dtype=jnp.int32)[None, :]
    ).astype(jnp.bfloat16)
    ranking = jnp.dot(earlier, onehot.astype(jnp.bfloat16), preferred_element_type=jnp.float32)
    slot = jnp.sum(jnp.where(onehot, ranking, 0.0), axis=1).astype(jnp.int32)
    position = chosen * capacity + slot
    pos2 = position.reshape(token_count, 2)
    iota_p = jnp.arange(places, dtype=jnp.int32)[:, None]
    pick0 = pos2[None, :, 0] == iota_p
    pick1 = pos2[None, :, 1] == iota_p
    kept = keep.astype(jnp.float32)
    scale = (gate_weights * kept).astype(jnp.bfloat16)
    slot_scale = (
        jnp.dot(pick0.astype(jnp.bfloat16), scale[:, 0], preferred_element_type=jnp.float32)
        + jnp.dot(pick1.astype(jnp.bfloat16), scale[:, 1], preferred_element_type=jnp.float32)
    ).astype(jnp.bfloat16).reshape(experts, local_experts, capacity)
    arrived_scale = lax.all_to_all(slot_scale, "expert", split_axis=0, concat_axis=2, tiled=True)
    weight = arrived_scale.reshape(local_experts, slot_count).astype(jnp.float32)
    gathered = ring_gather(out_grad, "tensor")
    full_weight = lax.all_gather(down_weight, "dp", axis=2, tiled=True)
    placing = (pick0 | pick1).astype(jnp.bfloat16).reshape(experts, local_experts, capacity, -1)
    half_width = gathered.shape[1] // 2
    dp_index = lax.axis_index("dp")
    grad_rows, scores_local, own_terms, peer_terms = [], [], [], []
    peer_hidden = from_partner(hidden_act, "dp", 0)
    for local in range(local_experts):
        outgoing = lax.dot_general(
            placing[:, local], gathered, (((2,), (0,)), ((), ())),
            preferred_element_type=jnp.float32,
        ).astype(jnp.bfloat16)
        routed = lax.all_to_all(
            outgoing, "expert", split_axis=0, concat_axis=0, tiled=True
        ).reshape(slot_count, -1)
        backprop = jnp.dot(routed, full_weight[local].T, preferred_element_type=jnp.float32)
        grad_rows.append((weight[local][:, None] * backprop).astype(jnp.bfloat16))
        scores_local.append(
            jnp.sum(backprop * hidden_act[local].astype(jnp.float32), axis=1)
        )
        scaled = (weight[local][:, None] * routed.astype(jnp.float32)).astype(jnp.bfloat16)
        own_cols = lax.dynamic_slice_in_dim(scaled, dp_index * half_width, half_width, 1)
        theirs = lax.dynamic_slice_in_dim(scaled, (1 - dp_index) * half_width, half_width, 1)
        peer_scaled = from_partner(theirs, "dp", 0)
        own_terms.append(
            jnp.dot(hidden_act[local].T, own_cols, preferred_element_type=jnp.float32).astype(
                jnp.bfloat16
            )
        )
        peer_terms.append(
            jnp.dot(peer_hidden[local].T, peer_scaled, preferred_element_type=jnp.float32).astype(
                jnp.bfloat16
            )
        )
    grad_hidden = jnp.stack(grad_rows)
    scores = tree_sum(jnp.stack(scores_local), "tensor")
    returned = lax.all_to_all(
        scores.reshape(local_experts, experts, capacity),
        "expert",
        split_axis=1,
        concat_axis=0,
        tiled=True,
    ).reshape(-1)
    picked = jnp.sum(
        jnp.where(position[:, None] == iota_p[None, :, 0], returned[None, :], 0.0), axis=1
    )
    gate_grad = picked.reshape(token_count, 2) * kept
    own_term, peer_term = lax.optimization_barrier((jnp.stack(own_terms), jnp.stack(peer_terms)))
    summed = own_term.astype(jnp.float32) + peer_term.astype(jnp.float32)
    grad_down = summed.astype(jnp.bfloat16)
    return (grad_down, grad_hidden, gate_grad)


def solution(mesh):
    in_specs = (
        P(("expert", "dp"), "tensor"),
        P(("expert", "dp"), None),
        P(("expert", "dp"), None),
        P(("expert", "dp"), None),
        P("expert", "dp", "tensor"),
        P("expert", "tensor", "dp"),
    )
    out_specs = (
        P("expert", "tensor", "dp"),
        P("expert", "dp", "tensor"),
        P(("expert", "dp"), None),
    )
    return jax.shard_map(body, mesh=mesh, in_specs=in_specs, out_specs=out_specs, check_vma=False)
```

```python
import jax
import jax.numpy as jnp
from jax import lax
from jax.sharding import PartitionSpec as P


def from_partner(value, axis, stride):
    mask = 2**stride
    pairs = [(source, source ^ mask) for source in range(lax.axis_size(axis))]
    return lax.ppermute(value, axis, pairs)


def tree_sum(value, axis):
    stride = 0
    while 2**stride < lax.axis_size(axis):
        value = value + from_partner(value, axis, stride)
        stride += 1
    return value


def ring_gather(value, axis):
    size = lax.axis_size(axis)
    index = lax.axis_index(axis)
    right = [(source, (source + 1) % size) for source in range(size)]
    left = [(source, (source - 1) % size) for source in range(size)]
    width = value.shape[1]
    gathered = jnp.zeros((value.shape[0], size * width), value.dtype)
    gathered = lax.dynamic_update_slice_in_dim(gathered, value, index * width, 1)
    going_right = going_left = value
    for step in range(1, size // 2 + 1):
        going_right = lax.ppermute(going_right, axis, right)
        gathered = lax.dynamic_update_slice_in_dim(
            gathered, going_right, (index + size - step) % size * width, 1
        )
        if step < size - size // 2:
            going_left = lax.ppermute(going_left, axis, left)
            gathered = lax.dynamic_update_slice_in_dim(
                gathered, going_left, (index + step) % size * width, 1
            )
    return gathered

def body(out_grad, expert_ids, gate_weights, keep, hidden_act, down_weight):
    token_count = out_grad.shape[0]
    experts = lax.axis_size("expert")
    local_experts = hidden_act.shape[0]
    total_experts = experts * local_experts
    slot_count = hidden_act.shape[1]
    capacity = slot_count // experts
    places = total_experts * capacity
    chosen = expert_ids.reshape(-1)
    count = chosen.shape[0]
    onehot = chosen[:, None] == jnp.arange(total_experts, dtype=jnp.int32)[None, :]
    earlier = (
        jnp.arange(count, dtype=jnp.int32)[:, None] > jnp.arange(count, dtype=jnp.int32)[None, :]
    ).astype(jnp.bfloat16)
    ranking = jnp.dot(earlier, onehot.astype(jnp.bfloat16), preferred_element_type=jnp.float32)
    slot = jnp.sum(jnp.where(onehot, ranking, 0.0), axis=1).astype(jnp.int32)
    position = chosen * capacity + slot
    pos2 = position.reshape(token_count, 2)
    iota_p = jnp.arange(places, dtype=jnp.int32)[:, None]
    pick0 = pos2[None, :, 0] == iota_p
    pick1 = pos2[None, :, 1] == iota_p
    kept = keep.astype(jnp.float32)
    scale = (gate_weights * kept).astype(jnp.bfloat16)
    slot_scale = (
        jnp.dot(pick0.astype(jnp.bfloat16), scale[:, 0], preferred_element_type=jnp.float32)
        + jnp.dot(pick1.astype(jnp.bfloat16), scale[:, 1], preferred_element_type=jnp.float32)
    ).astype(jnp.bfloat16).reshape(experts, local_experts, capacity)
    arrived_scale = lax.all_to_all(slot_scale, "expert", split_axis=0, concat_axis=2, tiled=True)
    weight = arrived_scale.reshape(local_experts, slot_count).astype(jnp.float32)
    gathered = ring_gather(out_grad, "tensor")
    full_weight = lax.all_gather(down_weight, "dp", axis=2, tiled=True)
    placing = (pick0 | pick1).astype(jnp.bfloat16).reshape(experts, local_experts, capacity, -1)
    half_width = gathered.shape[1] // 2
    dp_index = lax.axis_index("dp")
    grad_rows, scores_local, own_terms, peer_terms = [], [], [], []
    peer_hidden = from_partner(hidden_act, "dp", 0)
    for local in range(local_experts):
        outgoing = lax.dot_general(
            placing[:, local], gathered, (((2,), (0,)), ((), ())),
            preferred_element_type=jnp.float32,
        ).astype(jnp.bfloat16)
        routed = lax.all_to_all(
            outgoing, "expert", split_axis=0, concat_axis=0, tiled=True
        ).reshape(slot_count, -1)
        backprop = jnp.dot(routed, full_weight[local].T, preferred_element_type=jnp.float32)
        grad_rows.append((weight[local][:, None] * backprop).astype(jnp.bfloat16))
        scores_local.append(
            jnp.sum(backprop * hidden_act[local].astype(jnp.float32), axis=1)
        )
        scaled = (weight[local][:, None] * routed.astype(jnp.float32)).astype(jnp.bfloat16)
        own_cols = lax.dynamic_slice_in_dim(scaled, dp_index * half_width, half_width, 1)
        theirs = lax.dynamic_slice_in_dim(scaled, (1 - dp_index) * half_width, half_width, 1)
        peer_scaled = from_partner(theirs, "dp", 0)
        own_terms.append(
            jnp.dot(hidden_act[local].T, own_cols, preferred_element_type=jnp.float32).astype(
                jnp.bfloat16
            )
        )
        peer_terms.append(
            jnp.dot(peer_hidden[local].T, peer_scaled, preferred_element_type=jnp.float32).astype(
                jnp.bfloat16
            )
        )
    grad_hidden = jnp.stack(grad_rows)
    tensor_size = lax.axis_size("tensor")
    partial = jnp.stack(scores_local).reshape(local_experts, experts, capacity).transpose(1, 0, 2)
    outgoing_scores = jnp.broadcast_to(
        partial[:, None], (experts, tensor_size, local_experts, capacity)
    ).reshape(experts * tensor_size, local_experts, capacity)
    returned = lax.all_to_all(
        outgoing_scores, ("expert", "tensor"), split_axis=0, concat_axis=0, tiled=True
    )
    returned = jnp.sum(
        returned.reshape(experts, tensor_size, local_experts, capacity), axis=1
    ).reshape(-1)
    picked = jnp.sum(
        jnp.where(position[:, None] == iota_p[None, :, 0], returned[None, :], 0.0), axis=1
    )
    gate_grad = picked.reshape(token_count, 2) * kept
    own_term, peer_term = lax.optimization_barrier((jnp.stack(own_terms), jnp.stack(peer_terms)))
    summed = own_term.astype(jnp.float32) + peer_term.astype(jnp.float32)
    grad_down = summed.astype(jnp.bfloat16)
    return (grad_down, grad_hidden, gate_grad)


def solution(mesh):
    in_specs = (
        P(("expert", "dp"), "tensor"),
        P(("expert", "dp"), None),
        P(("expert", "dp"), None),
        P(("expert", "dp"), None),
        P("expert", "dp", "tensor"),
        P("expert", "tensor", "dp"),
    )
    out_specs = (
        P("expert", "tensor", "dp"),
        P("expert", "dp", "tensor"),
        P(("expert", "dp"), None),
    )
    return jax.shard_map(body, mesh=mesh, in_specs=in_specs, out_specs=out_specs, check_vma=False)
```

```python
import jax
import jax.numpy as jnp
from jax import lax
from jax.sharding import PartitionSpec as P


def from_partner(value, axis, stride):
    mask = 2**stride
    pairs = [(source, source ^ mask) for source in range(lax.axis_size(axis))]
    return lax.ppermute(value, axis, pairs)


def tree_sum(value, axis):
    stride = 0
    while 2**stride < lax.axis_size(axis):
        value = value + from_partner(value, axis, stride)
        stride += 1
    return value


def ring_gather(value, axis):
    size = lax.axis_size(axis)
    index = lax.axis_index(axis)
    right = [(source, (source + 1) % size) for source in range(size)]
    left = [(source, (source - 1) % size) for source in range(size)]
    width = value.shape[1]
    gathered = jnp.zeros((value.shape[0], size * width), value.dtype)
    gathered = lax.dynamic_update_slice_in_dim(gathered, value, index * width, 1)
    going_right = going_left = value
    for step in range(1, size // 2 + 1):
        going_right = lax.ppermute(going_right, axis, right)
        gathered = lax.dynamic_update_slice_in_dim(
            gathered, going_right, (index + size - step) % size * width, 1
        )
        if step < size - size // 2:
            going_left = lax.ppermute(going_left, axis, left)
            gathered = lax.dynamic_update_slice_in_dim(
                gathered, going_left, (index + step) % size * width, 1
            )
    return gathered

def body(out_grad, expert_ids, gate_weights, keep, hidden_act, down_weight):
    token_count = out_grad.shape[0]
    experts = lax.axis_size("expert")
    local_experts = hidden_act.shape[0]
    total_experts = experts * local_experts
    slot_count = hidden_act.shape[1]
    capacity = slot_count // experts
    places = total_experts * capacity
    chosen = expert_ids.reshape(-1)
    count = chosen.shape[0]
    onehot = chosen[:, None] == jnp.arange(total_experts, dtype=jnp.int32)[None, :]
    earlier = (
        jnp.arange(count, dtype=jnp.int32)[:, None] > jnp.arange(count, dtype=jnp.int32)[None, :]
    ).astype(jnp.bfloat16)
    ranking = jnp.dot(earlier, onehot.astype(jnp.bfloat16), preferred_element_type=jnp.float32)
    slot = jnp.sum(jnp.where(onehot, ranking, 0.0), axis=1).astype(jnp.int32)
    position = chosen * capacity + slot
    pos2 = position.reshape(token_count, 2)
    iota_p = jnp.arange(places, dtype=jnp.int32)[:, None]
    pick0 = pos2[None, :, 0] == iota_p
    pick1 = pos2[None, :, 1] == iota_p
    kept = keep.astype(jnp.float32)
    scale = (gate_weights * kept).astype(jnp.bfloat16)
    slot_scale = (
        jnp.dot(pick0.astype(jnp.bfloat16), scale[:, 0], preferred_element_type=jnp.float32)
        + jnp.dot(pick1.astype(jnp.bfloat16), scale[:, 1], preferred_element_type=jnp.float32)
    ).astype(jnp.bfloat16).reshape(experts, local_experts, capacity)
    arrived_scale = lax.all_to_all(slot_scale, "expert", split_axis=0, concat_axis=2, tiled=True)
    weight = arrived_scale.reshape(local_experts, slot_count).astype(jnp.float32)
    gathered = ring_gather(out_grad, "tensor")
    full_weight = lax.all_gather(down_weight, "dp", axis=2, tiled=True)
    placing = (pick0 | pick1).astype(jnp.bfloat16).reshape(experts, local_experts, capacity, -1)
    half_width = gathered.shape[1] // 2
    dp_index = lax.axis_index("dp")
    grad_rows, scores_local, own_terms, peer_terms = [], [], [], []
    peer_hidden = from_partner(hidden_act, "dp", 0)
    for local in range(local_experts):
        outgoing = lax.dot_general(
            placing[:, local], gathered, (((2,), (0,)), ((), ())),
            preferred_element_type=jnp.float32,
        ).astype(jnp.bfloat16)
        routed = lax.all_to_all(
            outgoing, "expert", split_axis=0, concat_axis=0, tiled=True
        ).reshape(slot_count, -1)
        backprop = jnp.dot(routed, full_weight[local].T, preferred_element_type=jnp.float32)
        grad_rows.append((weight[local][:, None] * backprop).astype(jnp.bfloat16))
        scores_local.append(
            jnp.sum(backprop * hidden_act[local].astype(jnp.float32), axis=1)
        )
        scaled = (weight[local][:, None] * routed.astype(jnp.float32)).astype(jnp.bfloat16)
        own_cols = lax.dynamic_slice_in_dim(scaled, dp_index * half_width, half_width, 1)
        theirs = lax.dynamic_slice_in_dim(scaled, (1 - dp_index) * half_width, half_width, 1)
        peer_scaled = from_partner(theirs, "dp", 0)
        own_terms.append(own_cols)
        peer_terms.append(peer_scaled)
    grad_hidden = jnp.stack(grad_rows)
    tensor_size = lax.axis_size("tensor")
    partial = jnp.stack(scores_local).reshape(local_experts, experts, capacity).transpose(1, 0, 2)
    outgoing_scores = jnp.broadcast_to(
        partial[:, None], (experts, tensor_size, local_experts, capacity)
    ).reshape(experts * tensor_size, local_experts, capacity)
    outgoing_scores, term_hidden, term_peer = lax.optimization_barrier(
        (outgoing_scores, hidden_act, peer_hidden)
    )
    for local in range(local_experts):
        own_terms[local] = jnp.dot(
            term_hidden[local].T, own_terms[local], preferred_element_type=jnp.float32
        ).astype(jnp.bfloat16)
        peer_terms[local] = jnp.dot(
            term_peer[local].T, peer_terms[local], preferred_element_type=jnp.float32
        ).astype(jnp.bfloat16)
    returned = lax.all_to_all(
        outgoing_scores, ("expert", "tensor"), split_axis=0, concat_axis=0, tiled=True
    )
    returned = jnp.sum(
        returned.reshape(experts, tensor_size, local_experts, capacity), axis=1
    ).reshape(-1)
    picked = jnp.sum(
        jnp.where(position[:, None] == iota_p[None, :, 0], returned[None, :], 0.0), axis=1
    )
    gate_grad = picked.reshape(token_count, 2) * kept
    own_term, peer_term = lax.optimization_barrier((jnp.stack(own_terms), jnp.stack(peer_terms)))
    summed = own_term.astype(jnp.float32) + peer_term.astype(jnp.float32)
    grad_down = summed.astype(jnp.bfloat16)
    return (grad_down, grad_hidden, gate_grad)


def solution(mesh):
    in_specs = (
        P(("expert", "dp"), "tensor"),
        P(("expert", "dp"), None),
        P(("expert", "dp"), None),
        P(("expert", "dp"), None),
        P("expert", "dp", "tensor"),
        P("expert", "tensor", "dp"),
    )
    out_specs = (
        P("expert", "tensor", "dp"),
        P("expert", "dp", "tensor"),
        P(("expert", "dp"), None),
    )
    return jax.shard_map(body, mesh=mesh, in_specs=in_specs, out_specs=out_specs, check_vma=False)
```

```python
import jax
import jax.numpy as jnp
from jax import lax
from jax.sharding import PartitionSpec as P


def from_partner(value, axis, stride):
    mask = 2**stride
    pairs = [(source, source ^ mask) for source in range(lax.axis_size(axis))]
    return lax.ppermute(value, axis, pairs)


def tree_sum(value, axis):
    stride = 0
    while 2**stride < lax.axis_size(axis):
        value = value + from_partner(value, axis, stride)
        stride += 1
    return value


def ring_gather(value, axis):
    size = lax.axis_size(axis)
    index = lax.axis_index(axis)
    right = [(source, (source + 1) % size) for source in range(size)]
    left = [(source, (source - 1) % size) for source in range(size)]
    width = value.shape[1]
    gathered = jnp.zeros((value.shape[0], size * width), value.dtype)
    gathered = lax.dynamic_update_slice_in_dim(gathered, value, index * width, 1)
    going_right = going_left = value
    for step in range(1, size // 2 + 1):
        going_right = lax.ppermute(going_right, axis, right)
        gathered = lax.dynamic_update_slice_in_dim(
            gathered, going_right, (index + size - step) % size * width, 1
        )
        if step < size - size // 2:
            going_left = lax.ppermute(going_left, axis, left)
            gathered = lax.dynamic_update_slice_in_dim(
                gathered, going_left, (index + step) % size * width, 1
            )
    return gathered

def body(out_grad, expert_ids, gate_weights, keep, hidden_act, down_weight):
    token_count = out_grad.shape[0]
    experts = lax.axis_size("expert")
    local_experts = hidden_act.shape[0]
    total_experts = experts * local_experts
    slot_count = hidden_act.shape[1]
    capacity = slot_count // experts
    places = total_experts * capacity
    chosen = expert_ids.reshape(-1)
    count = chosen.shape[0]
    onehot = chosen[:, None] == jnp.arange(total_experts, dtype=jnp.int32)[None, :]
    earlier = (
        jnp.arange(count, dtype=jnp.int32)[:, None] > jnp.arange(count, dtype=jnp.int32)[None, :]
    ).astype(jnp.bfloat16)
    ranking = jnp.dot(earlier, onehot.astype(jnp.bfloat16), preferred_element_type=jnp.float32)
    slot = jnp.sum(jnp.where(onehot, ranking, 0.0), axis=1).astype(jnp.int32)
    position = chosen * capacity + slot
    pos2 = position.reshape(token_count, 2)
    iota_p = jnp.arange(places, dtype=jnp.int32)[:, None]
    pick0 = pos2[None, :, 0] == iota_p
    pick1 = pos2[None, :, 1] == iota_p
    kept = keep.astype(jnp.float32)
    scale = (gate_weights * kept).astype(jnp.bfloat16)
    slot_scale = (
        jnp.dot(pick0.astype(jnp.bfloat16), scale[:, 0], preferred_element_type=jnp.float32)
        + jnp.dot(pick1.astype(jnp.bfloat16), scale[:, 1], preferred_element_type=jnp.float32)
    ).astype(jnp.bfloat16).reshape(experts, local_experts, capacity)
    arrived_scale = lax.all_to_all(slot_scale, "expert", split_axis=0, concat_axis=2, tiled=True)
    weight = arrived_scale.reshape(local_experts, slot_count).astype(jnp.float32)
    gathered = ring_gather(out_grad, "tensor")
    full_weight = lax.all_gather(down_weight, "dp", axis=2, tiled=True)
    placing = (pick0 | pick1).astype(jnp.bfloat16).reshape(experts, local_experts, capacity, -1)
    half_width = gathered.shape[1] // 2
    dp_index = lax.axis_index("dp")
    grad_rows, scores_local, own_terms, peer_terms = [], [], [], []
    peer_hidden = from_partner(hidden_act, "dp", 0)
    for local in range(local_experts):
        outgoing = lax.dot_general(
            placing[:, local], gathered, (((2,), (0,)), ((), ())),
            preferred_element_type=jnp.float32,
        ).astype(jnp.bfloat16)
        routed = lax.all_to_all(
            outgoing, "expert", split_axis=0, concat_axis=0, tiled=True
        ).reshape(slot_count, -1)
        backprop = jnp.dot(routed, full_weight[local].T, preferred_element_type=jnp.float32)
        grad_rows.append((weight[local][:, None] * backprop).astype(jnp.bfloat16))
        scores_local.append(
            jnp.sum(backprop * hidden_act[local].astype(jnp.float32), axis=1)
        )
        scaled = (weight[local][:, None] * routed.astype(jnp.float32)).astype(jnp.bfloat16)
        own_cols = lax.dynamic_slice_in_dim(scaled, dp_index * half_width, half_width, 1)
        theirs = lax.dynamic_slice_in_dim(scaled, (1 - dp_index) * half_width, half_width, 1)
        peer_scaled = from_partner(theirs, "dp", 0)
        own_terms.append(own_cols)
        peer_terms.append(peer_scaled)
    grad_hidden = jnp.stack(grad_rows)
    tensor_size = lax.axis_size("tensor")
    partial = jnp.stack(scores_local).reshape(local_experts, experts, capacity).transpose(1, 0, 2)
    outgoing_scores = jnp.broadcast_to(
        partial[:, None], (experts, tensor_size, local_experts, capacity)
    ).reshape(experts * tensor_size, local_experts, capacity)
    outgoing_scores, term_hidden, term_peer = lax.optimization_barrier(
        (outgoing_scores, hidden_act, peer_hidden)
    )
    for local in range(local_experts):
        own_terms[local] = jnp.dot(
            term_hidden[local].T, own_terms[local], preferred_element_type=jnp.float32
        ).astype(jnp.bfloat16)
    returned = lax.all_to_all(
        outgoing_scores, ("expert", "tensor"), split_axis=0, concat_axis=0, tiled=True
    )
    returned, term_peer = lax.optimization_barrier((returned, term_peer))
    for local in range(local_experts):
        peer_terms[local] = jnp.dot(
            term_peer[local].T, peer_terms[local], preferred_element_type=jnp.float32
        ).astype(jnp.bfloat16)
    returned = jnp.sum(
        returned.reshape(experts, tensor_size, local_experts, capacity), axis=1
    ).reshape(-1)
    picked = jnp.sum(
        jnp.where(position[:, None] == iota_p[None, :, 0], returned[None, :], 0.0), axis=1
    )
    gate_grad = picked.reshape(token_count, 2) * kept
    own_term, peer_term = lax.optimization_barrier((jnp.stack(own_terms), jnp.stack(peer_terms)))
    summed = own_term.astype(jnp.float32) + peer_term.astype(jnp.float32)
    grad_down = summed.astype(jnp.bfloat16)
    return (grad_down, grad_hidden, gate_grad)


def solution(mesh):
    in_specs = (
        P(("expert", "dp"), "tensor"),
        P(("expert", "dp"), None),
        P(("expert", "dp"), None),
        P(("expert", "dp"), None),
        P("expert", "dp", "tensor"),
        P("expert", "tensor", "dp"),
    )
    out_specs = (
        P("expert", "tensor", "dp"),
        P("expert", "dp", "tensor"),
        P(("expert", "dp"), None),
    )
    return jax.shard_map(body, mesh=mesh, in_specs=in_specs, out_specs=out_specs, check_vma=False)
```
